128 devices in a mesh: row: 8 (over z, core), col: 16 (over x, y).
Axes of the slice: x: 4, y: 4, z: 4, core: 2. Of those that a mesh axis runs over, the one named last changes fastest.
Arguments:
- page_tokens: bfloat16 [1024, 7168], P('row', 'col'), may hold values from -6 to 6
- weight_in: bfloat16 [7168, 28672], P('col', 'row'), may hold values from -0.0625 to 0.0625
- weight_out: bfloat16 [28672, 7168], P('row', 'col'), may hold values from -0.03125 to 0.03125
- upstream: bfloat16 [1024, 7168], P('row', 'col'), may hold values from -3 to 3
Outputs:
- block_out: bfloat16 [1024, 7168], P('row', 'col')
- grad_tokens: bfloat16 [1024, 7168], P('row', 'col')
- grad_weight_in: bfloat16 [7168, 28672], P('col', 'row')
- grad_weight_out: bfloat16 [28672, 7168], P('row', 'col')
The draws below stay inside these ranges and needn't reach their ends.
All inputs are finite; a program needn't handle non-finite values.
Results may differ from the reference program's by a relative error of at most 0.028.
Values may be sent and summed in bfloat16 or wider, within the bound.
No kernel may reach another device: no remote copies, remote signals or barrier semaphores. Data moves between devices by JAX's collectives and lax.ppermute only.
A program may use at most 128 MiB of HBM per device.

```python
import jax
import jax.numpy as jnp
from jax import lax

D = 7168
FF = 28672
TOKENS = 1024
N_ROW = 8
N_COL = 16


def block_levels(stream_key, dims, shards, smallest, top_value):
    factor_of = 1.0
    for axis_at, shards_of in shards:
        steps = jax.random.uniform(jax.random.fold_in(jax.random.fold_in(stream_key, 6), axis_at), (shards_of,), jnp.float32, smallest / len(shards), top_value / len(shards))
        factor_of = factor_of * jnp.repeat(jnp.exp(steps), dims[axis_at] // shards_of).reshape((-1,) + (1,) * (len(dims) - 1 - axis_at))
    return factor_of


def gaussian(own_key, dims, deviation, most, split=(), dtype=jnp.bfloat16):
    loudness = block_levels(own_key, dims, split, -0.22, 0.18) if split else 1.0
    values = jax.random.normal(own_key, dims, jnp.float32) * deviation * loudness
    return jnp.minimum(jnp.maximum(values, -most), most).astype(dtype)


def setup_inputs(seed: int = 0) -> dict:
    arg_keys = jax.random.split(jax.random.key(seed), 5)
    return {
        "page_tokens": gaussian(arg_keys[0], (TOKENS, D), 1.0, 6.0, ((0, 8), (1, 16))),
        "weight_in": gaussian(arg_keys[1], (D, FF), D ** -0.5, 0.0625, ((0, 16), (1, 8))),
        "weight_out": gaussian(arg_keys[2], (FF, D), FF ** -0.5, 0.03125, ((0, 8), (1, 16))),
        "upstream": gaussian(arg_keys[3], (TOKENS, D), 0.5, 3.0, ((0, 8), (1, 16))),
    }


def activate(values):
    return 0.5 * values * (1.0 + jnp.tanh(0.7978845608 * (values + 0.044715 * values * values * values)))

def partial_sums(left, right, parts):
    stride = left.shape[1] // parts
    total = jnp.zeros((left.shape[0], right.shape[1]), jnp.float32)
    for index in range(parts):
        piece = jnp.dot(left[:, index * stride:(index + 1) * stride], right[index * stride:(index + 1) * stride, :], preferred_element_type=jnp.float32)
        piece = lax.optimization_barrier(piece.astype(jnp.bfloat16))
        total = total + piece.astype(jnp.float32)
    return total

def reference(page_tokens, weight_in, weight_out, upstream):
    hidden_pre = partial_sums(page_tokens, weight_in, N_COL)
    active = activate(hidden_pre).astype(jnp.bfloat16)
    block_out = partial_sums(active, weight_out, N_ROW).astype(jnp.bfloat16)
    grad_active = partial_sums(upstream, weight_out.T, N_COL)
    grad_hidden = jax.vjp(activate, hidden_pre)[1](grad_active)[0].astype(jnp.bfloat16)
    grad_tokens = partial_sums(grad_hidden, weight_in.T, N_ROW).astype(jnp.bfloat16)
    grad_weight_in = jnp.dot(page_tokens.T, grad_hidden, preferred_element_type=jnp.float32).astype(jnp.bfloat16)
    grad_weight_out = jnp.dot(active.T, upstream, preferred_element_type=jnp.float32).astype(jnp.bfloat16)
    return (block_out, grad_tokens, grad_weight_in, grad_weight_out)
```

```python
import jax
import jax.numpy as jnp
from jax import lax
from jax.sharding import Mesh
from jax.sharding import PartitionSpec as P

ROW = ("z", "core")
COL = ("x", "y")


def activate(values):
    return (
        0.5
        * values
        * (1.0 + jnp.tanh(0.7978845608 * (values + 0.044715 * values * values * values)))
    )


def activate_back(values, grads):
    return jax.vjp(activate, values)[1](grads)[0]


def contract_last(left, right):
    return lax.dot_general(
        left, right, (((1,), (1,)), ((), ())), preferred_element_type=jnp.float32
    )


def contract_first(left, right):
    return lax.dot_general(
        left, right, (((0,), (0,)), ((), ())), preferred_element_type=jnp.float32
    )


def ring_rs(blocks, ax, n, d):
    i = lax.axis_index(ax)
    perm = [(j, (j + d) % n) for j in range(n)]
    acc = lax.dynamic_index_in_dim(blocks, (i - d) % n, 0, keepdims=False)
    for s in range(1, n):
        acc = lax.ppermute(acc, ax, perm)
        acc = acc + lax.dynamic_index_in_dim(blocks, (i - d * (s + 1)) % n, 0, keepdims=False)
    return acc


def ring_ag(b, ax, n, d):
    i = lax.axis_index(ax)
    perm = [(j, (j + d) % n) for j in range(n)]
    out = jnp.zeros((n,) + b.shape, b.dtype)
    out = lax.dynamic_update_index_in_dim(out, b, i, 0)
    cur = b
    for s in range(1, n):
        cur = lax.ppermute(cur, ax, perm)
        out = lax.dynamic_update_index_in_dim(out, cur, (i - d * s) % n, 0)
    return out


def direct_ag(b, ax, n):
    i = lax.axis_index(ax)
    out = jnp.zeros((n,) + b.shape, b.dtype)
    out = lax.dynamic_update_index_in_dim(out, b, i, 0)
    for s in range(1, n):
        perm = [(j, (j + s) % n) for j in range(n)]
        out = lax.dynamic_update_index_in_dim(out, lax.ppermute(b, ax, perm), (i - s) % n, 0)
    return out


def direct_rs(blocks, ax, n):
    i = lax.axis_index(ax)
    acc = lax.dynamic_index_in_dim(blocks, i, 0, keepdims=False).astype(jnp.float32)
    for s in range(1, n):
        perm = [(j, (j + s) % n) for j in range(n)]
        send = lax.dynamic_index_in_dim(blocks, (i + s) % n, 0, keepdims=False)
        acc = acc + lax.ppermute(send, ax, perm).astype(jnp.float32)
    return acc


def to_ring_order(a):
    a5 = a.reshape(4, 4, 4, 16, a.shape[-1])
    pieces = []
    for q in range(4):
        piece = a5[:, :, q]
        if q >= 2:
            piece = piece.transpose(1, 0, 2, 3)
        pieces.append(piece.reshape(256, a.shape[-1]))
    return jnp.concatenate(pieces, 0)


def from_ring_order(a):
    pieces = []
    for q in range(4):
        piece = a[q * 256:(q + 1) * 256].reshape(4, 4, 16, a.shape[-1])
        if q >= 2:
            piece = piece.transpose(1, 0, 2, 3)
        pieces.append(piece)
    return jnp.stack(pieces, 2).reshape(a.shape)


def ring_scatter_col(a):
    qs = a.reshape(4, 4, 4, 16, a.shape[-1])
    outs = []
    for q in range(4):
        first, second = ("x", "y") if q < 2 else ("y", "x")
        d = 1 if q % 2 == 0 else -1
        r = ring_rs(qs[q], first, 4, d)
        r = ring_rs(r, second, 4, d)
        outs.append(r)
    return jnp.concatenate(outs, 0)


def ring_gather_col(b):
    parts = b.reshape(4, 16, b.shape[-1])
    outs = []
    for q in range(4):
        first, second = ("x", "y") if q < 2 else ("y", "x")
        d = 1 if q % 2 == 0 else -1
        g = ring_ag(parts[q], second, 4, d)
        g = ring_ag(g, first, 4, d)
        outs.append(g.reshape(256, b.shape[-1]))
    return jnp.concatenate(outs, 0)


def gather_row(b):
    g = direct_ag(b, "core", 2)
    g = direct_ag(g, "z", 4)
    return g.reshape((-1, b.shape[-1]))


def scatter_row(part):
    p4 = part.reshape(4, 2, part.shape[0] // 8, part.shape[-1])
    acc = direct_rs(p4, "z", 4)
    c = lax.axis_index("core")
    mine = lax.dynamic_index_in_dim(acc, c, 0, keepdims=False)
    other = lax.dynamic_index_in_dim(acc, 1 - c, 0, keepdims=False)
    return (mine + lax.ppermute(other, "core", [(0, 1), (1, 0)])).astype(jnp.bfloat16)


def shards(page_tokens, weight_in, weight_out, upstream):
    features = gather_row(page_tokens)
    upstream_all = gather_row(upstream)
    hidden_pre = lax.psum_scatter(
        jnp.dot(features, weight_in, preferred_element_type=jnp.float32).astype(jnp.bfloat16),
        COL,
        scatter_dimension=0,
        tiled=True,
    ).astype(jnp.float32)
    grad_active = ring_scatter_col(
        contract_last(to_ring_order(upstream_all), weight_out).astype(jnp.bfloat16)
    ).astype(jnp.float32)
    active = lax.all_gather(activate(hidden_pre).astype(jnp.bfloat16), COL, axis=0, tiled=True)
    grad_hidden = ring_gather_col(activate_back(hidden_pre, grad_active).astype(jnp.bfloat16))
    block_out = scatter_row(
        jnp.dot(active, weight_out, preferred_element_type=jnp.float32).astype(jnp.bfloat16)
    )
    grad_tokens = scatter_row(
        from_ring_order(contract_last(grad_hidden, weight_in).astype(jnp.bfloat16))
    )
    grad_weight_in = contract_first(to_ring_order(features), grad_hidden).astype(jnp.bfloat16)
    grad_weight_out = contract_first(active, upstream_all).astype(jnp.bfloat16)
    return (block_out, grad_tokens, grad_weight_in, grad_weight_out)


def solution(mesh):
    grid = Mesh(mesh.devices.reshape(mesh.shape["row"] // 2, 2, 4, mesh.shape["col"] // 4), ROW + COL)
    tok = P(ROW, COL)
    return jax.shard_map(
        shards,
        mesh=grid,
        in_specs=(tok, P(COL, ROW), tok, tok),
        out_specs=(tok, tok, P(COL, ROW), tok),
        check_vma=False,
    )
```

```python
import jax
import jax.numpy as jnp
from jax import lax
from jax.sharding import Mesh
from jax.sharding import PartitionSpec as P

ROW = ("z", "core")
COL = ("x", "y")


def activate(values):
    return (
        0.5
        * values
        * (1.0 + jnp.tanh(0.7978845608 * (values + 0.044715 * values * values * values)))
    )


def activate_back(values, grads):
    return jax.vjp(activate, values)[1](grads)[0]


def contract_last(left, right):
    return lax.dot_general(
        left, right, (((1,), (1,)), ((), ())), preferred_element_type=jnp.float32
    )


def contract_first(left, right):
    return lax.dot_general(
        left, right, (((0,), (0,)), ((), ())), preferred_element_type=jnp.float32
    )


def ring_rs(blocks, ax, n, d):
    i = lax.axis_index(ax)
    perm = [(j, (j + d) % n) for j in range(n)]
    acc = lax.dynamic_index_in_dim(blocks, (i - d) % n, 0, keepdims=False)
    for s in range(1, n):
        acc = lax.ppermute(acc, ax, perm)
        acc = acc + lax.dynamic_index_in_dim(blocks, (i - d * (s + 1)) % n, 0, keepdims=False)
    return acc


def ring_ag(b, ax, n, d):
    i = lax.axis_index(ax)
    perm = [(j, (j + d) % n) for j in range(n)]
    out = jnp.zeros((n,) + b.shape, b.dtype)
    out = lax.dynamic_update_index_in_dim(out, b, i, 0)
    cur = b
    for s in range(1, n):
        cur = lax.ppermute(cur, ax, perm)
        out = lax.dynamic_update_index_in_dim(out, cur, (i - d * s) % n, 0)
    return out


def direct_ag(b, ax, n):
    i = lax.axis_index(ax)
    out = jnp.zeros((n,) + b.shape, b.dtype)
    out = lax.dynamic_update_index_in_dim(out, b, i, 0)
    for s in range(1, n):
        perm = [(j, (j + s) % n) for j in range(n)]
        out = lax.dynamic_update_index_in_dim(out, lax.ppermute(b, ax, perm), (i - s) % n, 0)
    return out


def direct_rs(blocks, ax, n):
    i = lax.axis_index(ax)
    acc = lax.dynamic_index_in_dim(blocks, i, 0, keepdims=False).astype(jnp.float32)
    for s in range(1, n):
        perm = [(j, (j + s) % n) for j in range(n)]
        send = lax.dynamic_index_in_dim(blocks, (i + s) % n, 0, keepdims=False)
        acc = acc + lax.ppermute(send, ax, perm).astype(jnp.float32)
    return acc


def to_ring_order(a):
    a5 = a.reshape(4, 4, 4, 16, a.shape[-1])
    pieces = []
    for q in range(4):
        piece = a5[:, :, q]
        if q >= 2:
            piece = piece.transpose(1, 0, 2, 3)
        pieces.append(piece.reshape(256, a.shape[-1]))
    return jnp.concatenate(pieces, 0)


def from_ring_order(a):
    pieces = []
    for q in range(4):
        piece = a[q * 256:(q + 1) * 256].reshape(4, 4, 16, a.shape[-1])
        if q >= 2:
            piece = piece.transpose(1, 0, 2, 3)
        pieces.append(piece)
    return jnp.stack(pieces, 2).reshape(a.shape)


def ring_scatter_col(a):
    qs = a.reshape(4, 4, 4, 16, a.shape[-1])
    r = [ring_rs(qs[q], "x" if q < 2 else "y", 4, 1 if q % 2 == 0 else -1) for q in range(4)]
    low = ring_rs(jnp.stack(r[:2], 1), "y", 4, 1)
    high = ring_rs(jnp.stack(r[2:], 1), "x", 4, -1)
    return jnp.concatenate([low, high], 0).reshape(64, a.shape[-1])


def ring_gather_col(b):
    parts = b.reshape(2, 2, 16, b.shape[-1])
    low = ring_ag(parts[0], "y", 4, 1)
    high = ring_ag(parts[1], "x", 4, -1)
    outs = []
    for q in range(4):
        g = (low if q < 2 else high)[:, q % 2]
        g = ring_ag(g, "x" if q < 2 else "y", 4, 1 if q % 2 == 0 else -1)
        outs.append(g.reshape(256, b.shape[-1]))
    return jnp.concatenate(outs, 0)


def gather_row(b):
    g = direct_ag(b, "core", 2)
    g = direct_ag(g, "z", 4)
    return g.reshape((-1, b.shape[-1]))


def scatter_row(part):
    p4 = part.reshape(4, 2, part.shape[0] // 8, part.shape[-1])
    acc = direct_rs(p4, "z", 4)
    c = lax.axis_index("core")
    mine = lax.dynamic_index_in_dim(acc, c, 0, keepdims=False)
    other = lax.dynamic_index_in_dim(acc, 1 - c, 0, keepdims=False)
    return (mine + lax.ppermute(other, "core", [(0, 1), (1, 0)])).astype(jnp.bfloat16)


def shards(page_tokens, weight_in, weight_out, upstream):
    width = page_tokens.shape[1]
    both = gather_row(jnp.concatenate([page_tokens, upstream], 1))
    features = both[:, :width]
    upstream_all = both[:, width:]
    hidden_pre = lax.psum_scatter(
        jnp.dot(features, weight_in, preferred_element_type=jnp.float32).astype(jnp.bfloat16),
        COL,
        scatter_dimension=0,
        tiled=True,
    ).astype(jnp.float32)
    grad_active = ring_scatter_col(
        contract_last(to_ring_order(upstream_all), weight_out).astype(jnp.bfloat16)
    ).astype(jnp.float32)
    active = lax.all_gather(activate(hidden_pre).astype(jnp.bfloat16), COL, axis=0, tiled=True)
    grad_hidden = ring_gather_col(activate_back(hidden_pre, grad_active).astype(jnp.bfloat16))
    out_part = jnp.dot(active, weight_out, preferred_element_type=jnp.float32).astype(jnp.bfloat16)
    tokens_part = from_ring_order(contract_last(grad_hidden, weight_in).astype(jnp.bfloat16))
    outs = scatter_row(jnp.concatenate([out_part, tokens_part], 1))
    block_out = outs[:, :width]
    grad_tokens = outs[:, width:]
    grad_weight_in = contract_first(to_ring_order(features), grad_hidden).astype(jnp.bfloat16)
    grad_weight_out = contract_first(active, upstream_all).astype(jnp.bfloat16)
    return (block_out, grad_tokens, grad_weight_in, grad_weight_out)


def solution(mesh):
    grid = Mesh(mesh.devices.reshape(mesh.shape["row"] // 2, 2, 4, mesh.shape["col"] // 4), ROW + COL)
    tok = P(ROW, COL)
    return jax.shard_map(
        shards,
        mesh=grid,
        in_specs=(tok, P(COL, ROW), tok, tok),
        out_specs=(tok, tok, P(COL, ROW), tok),
        check_vma=False,
    )
```

```python
import jax
import jax.numpy as jnp
from jax import lax
from jax.sharding import Mesh
from jax.sharding import PartitionSpec as P

ROW = ("z", "core")
COL = ("x", "y")


def activate(values):
    return (
        0.5
        * values
        * (1.0 + jnp.tanh(0.7978845608 * (values + 0.044715 * values * values * values)))
    )


def activate_back(values, grads):
    return jax.vjp(activate, values)[1](grads)[0]


def contract_last(left, right):
    return lax.dot_general(
        left, right, (((1,), (1,)), ((), ())), preferred_element_type=jnp.float32
    )


def contract_first(left, right):
    return lax.dot_general(
        left, right, (((0,), (0,)), ((), ())), preferred_element_type=jnp.float32
    )


def ring_rs(blocks, ax, n, d):
    i = lax.axis_index(ax)
    perm = [(j, (j + d) % n) for j in range(n)]
    acc = lax.dynamic_index_in_dim(blocks, (i - d) % n, 0, keepdims=False)
    for s in range(1, n):
        acc = lax.ppermute(acc, ax, perm)
        acc = acc + lax.dynamic_index_in_dim(blocks, (i - d * (s + 1)) % n, 0, keepdims=False)
    return acc


def ring_ag(b, ax, n, d):
    i = lax.axis_index(ax)
    perm = [(j, (j + d) % n) for j in range(n)]
    out = jnp.zeros((n,) + b.shape, b.dtype)
    out = lax.dynamic_update_index_in_dim(out, b, i, 0)
    cur = b
    for s in range(1, n):
        cur = lax.ppermute(cur, ax, perm)
        out = lax.dynamic_update_index_in_dim(out, cur, (i - d * s) % n, 0)
    return out


def direct_ag(b, ax, n):
    i = lax.axis_index(ax)
    out = jnp.zeros((n,) + b.shape, b.dtype)
    out = lax.dynamic_update_index_in_dim(out, b, i, 0)
    for s in range(1, n):
        perm = [(j, (j + s) % n) for j in range(n)]
        out = lax.dynamic_update_index_in_dim(out, lax.ppermute(b, ax, perm), (i - s) % n, 0)
    return out


def direct_rs(blocks, ax, n):
    i = lax.axis_index(ax)
    acc = lax.dynamic_index_in_dim(blocks, i, 0, keepdims=False).astype(jnp.float32)
    for s in range(1, n):
        perm = [(j, (j + s) % n) for j in range(n)]
        send = lax.dynamic_index_in_dim(blocks, (i + s) % n, 0, keepdims=False)
        acc = acc + lax.ppermute(send, ax, perm).astype(jnp.float32)
    return acc


def to_ring_order(a):
    a5 = a.reshape(4, 4, 4, 16, a.shape[-1])
    pieces = []
    for q in range(4):
        piece = a5[:, :, q]
        if q >= 2:
            piece = piece.transpose(1, 0, 2, 3)
        pieces.append(piece.reshape(256, a.shape[-1]))
    return jnp.concatenate(pieces, 0)


def from_ring_order(a):
    pieces = []
    for q in range(4):
        piece = a[q * 256:(q + 1) * 256].reshape(4, 4, 16, a.shape[-1])
        if q >= 2:
            piece = piece.transpose(1, 0, 2, 3)
        pieces.append(piece)
    return jnp.stack(pieces, 2).reshape(a.shape)


def ring_scatter_col(a):
    qs = a.reshape(4, 4, 4, 16, a.shape[-1])
    r = [ring_rs(qs[q], "x" if q < 2 else "y", 4, 1 if q % 2 == 0 else -1) for q in range(4)]
    low = ring_rs(jnp.stack(r[:2], 1), "y", 4, 1)
    high = ring_rs(jnp.stack(r[2:], 1), "x", 4, -1)
    return jnp.concatenate([low, high], 0).reshape(64, a.shape[-1])


def ring_gather_col(b):
    parts = b.reshape(2, 2, 16, b.shape[-1])
    low = ring_ag(parts[0], "y", 4, 1)
    high = ring_ag(parts[1], "x", 4, -1)
    outs = []
    for q in range(4):
        g = (low if q < 2 else high)[:, q % 2]
        g = ring_ag(g, "x" if q < 2 else "y", 4, 1 if q % 2 == 0 else -1)
        outs.append(g.reshape(256, b.shape[-1]))
    return jnp.concatenate(outs, 0)


def gather_row(b):
    g = direct_ag(b, "core", 2)
    g = direct_ag(g, "z", 4)
    return g.reshape((-1, b.shape[-1]))


def scatter_row(part):
    p4 = part.reshape(4, 2, part.shape[0] // 8, part.shape[-1])
    acc = direct_rs(p4, "z", 4)
    c = lax.axis_index("core")
    mine = lax.dynamic_index_in_dim(acc, c, 0, keepdims=False)
    other = lax.dynamic_index_in_dim(acc, 1 - c, 0, keepdims=False)
    return (mine + lax.ppermute(other, "core", [(0, 1), (1, 0)])).astype(jnp.bfloat16)


def shards(page_tokens, weight_in, weight_out, upstream):
    width = page_tokens.shape[1]
    both = to_ring_order(gather_row(jnp.concatenate([page_tokens, upstream], 1)))
    features = both[:, :width]
    upstream_all = both[:, width:]
    hidden_pre = lax.psum(
        jnp.dot(features, weight_in, preferred_element_type=jnp.float32).astype(jnp.bfloat16),
        COL,
    ).astype(jnp.float32)
    grad_active = ring_gather_col(
        ring_scatter_col(contract_last(upstream_all, weight_out).astype(jnp.bfloat16))
    ).astype(jnp.float32)
    active = activate(hidden_pre).astype(jnp.bfloat16)
    grad_hidden = activate_back(hidden_pre, grad_active).astype(jnp.bfloat16)
    out_part = jnp.dot(active, weight_out, preferred_element_type=jnp.float32).astype(jnp.bfloat16)
    tokens_part = contract_last(grad_hidden, weight_in).astype(jnp.bfloat16)
    outs = scatter_row(from_ring_order(jnp.concatenate([out_part, tokens_part], 1)))
    block_out = outs[:, :width]
    grad_tokens = outs[:, width:]
    grad_weight_in = contract_first(features, grad_hidden).astype(jnp.bfloat16)
    grad_weight_out = contract_first(active, upstream_all).astype(jnp.bfloat16)
    return (block_out, grad_tokens, grad_weight_in, grad_weight_out)


def solution(mesh):
    grid = Mesh(mesh.devices.reshape(mesh.shape["row"] // 2, 2, 4, mesh.shape["col"] // 4), ROW + COL)
    tok = P(ROW, COL)
    return jax.shard_map(
        shards,
        mesh=grid,
        in_specs=(tok, P(COL, ROW), tok, tok),
        out_specs=(tok, tok, P(COL, ROW), tok),
        check_vma=False,
    )
```

```python
import jax
import jax.numpy as jnp
from jax import lax
from jax.sharding import Mesh
from jax.sharding import PartitionSpec as P

ROW = ("z", "core")
COL = ("x", "y")


def activate(values):
    return (
        0.5
        * values
        * (1.0 + jnp.tanh(0.7978845608 * (values + 0.044715 * values * values * values)))
    )


def activate_back(values, grads):
    return jax.vjp(activate, values)[1](grads)[0]


def contract_last(left, right):
    return lax.dot_general(
        left, right, (((1,), (1,)), ((), ())), preferred_element_type=jnp.float32
    )


def contract_first(left, right):
    return lax.dot_general(
        left, right, (((0,), (0,)), ((), ())), preferred_element_type=jnp.float32
    )


def ring_rs(blocks, ax, n, d):
    i = lax.axis_index(ax)
    perm = [(j, (j + d) % n) for j in range(n)]
    acc = lax.dynamic_index_in_dim(blocks, (i - d) % n, 0, keepdims=False)
    for s in range(1, n):
        acc = lax.ppermute(acc, ax, perm)
        acc = acc + lax.dynamic_index_in_dim(blocks, (i - d * (s + 1)) % n, 0, keepdims=False)
    return acc


def ring_ag(b, ax, n, d):
    i = lax.axis_index(ax)
    perm = [(j, (j + d) % n) for j in range(n)]
    out = jnp.zeros((n,) + b.shape, b.dtype)
    out = lax.dynamic_update_index_in_dim(out, b, i, 0)
    cur = b
    for s in range(1, n):
        cur = lax.ppermute(cur, ax, perm)
        out = lax.dynamic_update_index_in_dim(out, cur, (i - d * s) % n, 0)
    return out


def direct_ag(b, ax, n):
    i = lax.axis_index(ax)
    out = jnp.zeros((n,) + b.shape, b.dtype)
    out = lax.dynamic_update_index_in_dim(out, b, i, 0)
    for s in range(1, n):
        perm = [(j, (j + s) % n) for j in range(n)]
        out = lax.dynamic_update_index_in_dim(out, lax.ppermute(b, ax, perm), (i - s) % n, 0)
    return out


def direct_rs(blocks, ax, n):
    i = lax.axis_index(ax)
    acc = lax.dynamic_index_in_dim(blocks, i, 0, keepdims=False).astype(jnp.float32)
    for s in range(1, n):
        perm = [(j, (j + s) % n) for j in range(n)]
        send = lax.dynamic_index_in_dim(blocks, (i + s) % n, 0, keepdims=False)
        acc = acc + lax.ppermute(send, ax, perm).astype(jnp.float32)
    return acc


def to_ring_order(a):
    a5 = a.reshape(4, 4, 4, 16, a.shape[-1])
    pieces = []
    for q in range(4):
        piece = a5[:, :, q]
        if q >= 2:
            piece = piece.transpose(1, 0, 2, 3)
        pieces.append(piece.reshape(256, a.shape[-1]))
    return jnp.concatenate(pieces, 0)


def from_ring_order(a):
    pieces = []
    for q in range(4):
        piece = a[q * 256:(q + 1) * 256].reshape(4, 4, 16, a.shape[-1])
        if q >= 2:
            piece = piece.transpose(1, 0, 2, 3)
        pieces.append(piece)
    return jnp.stack(pieces, 2).reshape(a.shape)


def ring_scatter_col(a):
    qs = a.reshape(4, 4, 4, 16, a.shape[-1])
    r = [ring_rs(qs[q], "x" if q < 2 else "y", 4, 1 if q % 2 == 0 else -1) for q in range(4)]
    low = ring_rs(jnp.stack(r[:2], 1), "y", 4, 1)
    high = ring_rs(jnp.stack(r[2:], 1), "x", 4, -1)
    return jnp.concatenate([low, high], 0).reshape(64, a.shape[-1])


def ring_gather_col(b):
    parts = b.reshape(2, 2, 16, b.shape[-1])
    low = ring_ag(parts[0], "y", 4, 1)
    high = ring_ag(parts[1], "x", 4, -1)
    outs = []
    for q in range(4):
        g = (low if q < 2 else high)[:, q % 2]
        g = ring_ag(g, "x" if q < 2 else "y", 4, 1 if q % 2 == 0 else -1)
        outs.append(g.reshape(256, b.shape[-1]))
    return jnp.concatenate(outs, 0)


def relay_ag(b, ax):
    i = lax.axis_index(ax)
    fwd = [(j, (j + 1) % 4) for j in range(4)]
    bwd = [(j, (j - 1) % 4) for j in range(4)]
    half = b.shape[1] // 2
    from_left = lax.ppermute(b, ax, fwd)
    from_right = lax.ppermute(b, ax, bwd)
    far = jnp.concatenate(
        [lax.ppermute(from_left[:, :half], ax, fwd), lax.ppermute(from_right[:, half:], ax, bwd)], 1
    )
    out = jnp.zeros((4,) + b.shape, b.dtype)
    out = lax.dynamic_update_index_in_dim(out, b, i, 0)
    out = lax.dynamic_update_index_in_dim(out, from_left, (i - 1) % 4, 0)
    out = lax.dynamic_update_index_in_dim(out, from_right, (i + 1) % 4, 0)
    return lax.dynamic_update_index_in_dim(out, far, (i + 2) % 4, 0)


def relay_rs(blocks, ax):
    i = lax.axis_index(ax)
    fwd = [(j, (j + 1) % 4) for j in range(4)]
    bwd = [(j, (j - 1) % 4) for j in range(4)]
    rows = blocks.shape[2]
    half = rows // 2
    blk = lambda k: lax.dynamic_index_in_dim(blocks, (i + k) % 4, 0, keepdims=False)
    far = blk(2)
    recv_l = lax.ppermute(jnp.concatenate([blk(1), far[:, :half]], 1), ax, fwd)
    recv_r = lax.ppermute(jnp.concatenate([blk(3), far[:, half:]], 1), ax, bwd)
    far_in = jnp.concatenate(
        [lax.ppermute(recv_l[:, rows:], ax, fwd), lax.ppermute(recv_r[:, rows:], ax, bwd)], 1
    )
    f32 = jnp.float32
    return (
        blk(0).astype(f32)
        + recv_l[:, :rows].astype(f32)
        + recv_r[:, :rows].astype(f32)
        + far_in.astype(f32)
    )


def gather_row(b):
    g = direct_ag(b, "core", 2)
    g = relay_ag(g, "z")
    return g.reshape((-1, b.shape[-1]))


def scatter_row(part):
    p4 = part.reshape(4, 2, part.shape[0] // 8, part.shape[-1])
    acc = relay_rs(p4, "z")
    c = lax.axis_index("core")
    mine = lax.dynamic_index_in_dim(acc, c, 0, keepdims=False)
    other = lax.dynamic_index_in_dim(acc, 1 - c, 0, keepdims=False)
    return (mine + lax.ppermute(other, "core", [(0, 1), (1, 0)])).astype(jnp.bfloat16)


def shards(page_tokens, weight_in, weight_out, upstream):
    width = page_tokens.shape[1]
    both = gather_row(jnp.concatenate([page_tokens, upstream], 1))
    features = both[:, :width]
    upstream_all = both[:, width:]
    hidden_pre = lax.psum_scatter(
        jnp.dot(features, weight_in, preferred_element_type=jnp.float32).astype(jnp.bfloat16),
        COL,
        scatter_dimension=0,
        tiled=True,
    ).astype(jnp.float32)
    grad_active = ring_scatter_col(
        contract_last(to_ring_order(upstream_all), weight_out).astype(jnp.bfloat16)
    ).astype(jnp.float32)
    active = lax.all_gather(activate(hidden_pre).astype(jnp.bfloat16), COL, axis=0, tiled=True)
    grad_hidden = ring_gather_col(activate_back(hidden_pre, grad_active).astype(jnp.bfloat16))
    out_part = jnp.dot(active, weight_out, preferred_element_type=jnp.float32).astype(jnp.bfloat16)
    tokens_part = from_ring_order(contract_last(grad_hidden, weight_in).astype(jnp.bfloat16))
    outs = scatter_row(jnp.concatenate([out_part, tokens_part], 1))
    block_out = outs[:, :width]
    grad_tokens = outs[:, width:]
    grad_weight_in = contract_first(to_ring_order(features), grad_hidden).astype(jnp.bfloat16)
    grad_weight_out = contract_first(active, upstream_all).astype(jnp.bfloat16)
    return (block_out, grad_tokens, grad_weight_in, grad_weight_out)


def solution(mesh):
    grid = Mesh(mesh.devices.reshape(mesh.shape["row"] // 2, 2, 4, mesh.shape["col"] // 4), ROW + COL)
    tok = P(ROW, COL)
    return jax.shard_map(
        shards,
        mesh=grid,
        in_specs=(tok, P(COL, ROW), tok, tok),
        out_specs=(tok, tok, P(COL, ROW), tok),
        check_vma=False,
    )
```

```python
import jax
import jax.numpy as jnp
from jax import lax
from jax.sharding import Mesh
from jax.sharding import PartitionSpec as P

ROW = ("z", "core")
COL = ("x", "y")


def activate(values):
    return (
        0.5
        * values
        * (1.0 + jnp.tanh(0.7978845608 * (values + 0.044715 * values * values * values)))
    )


def activate_back(values, grads):
    return jax.vjp(activate, values)[1](grads)[0]


def contract_last(left, right):
    return lax.dot_general(
        left, right, (((1,), (1,)), ((), ())), preferred_element_type=jnp.float32
    )


def contract_first(left, right):
    return lax.dot_general(
        left, right, (((0,), (0,)), ((), ())), preferred_element_type=jnp.float32
    )


def ring_rs(blocks, ax, n, d):
    i = lax.axis_index(ax)
    perm = [(j, (j + d) % n) for j in range(n)]
    acc = lax.dynamic_index_in_dim(blocks, (i - d) % n, 0, keepdims=False)
    for s in range(1, n):
        acc = lax.ppermute(acc, ax, perm)
        acc = acc + lax.dynamic_index_in_dim(blocks, (i - d * (s + 1)) % n, 0, keepdims=False)
    return acc


def ring_ag(b, ax, n, d):
    i = lax.axis_index(ax)
    perm = [(j, (j + d) % n) for j in range(n)]
    out = jnp.zeros((n,) + b.shape, b.dtype)
    out = lax.dynamic_update_index_in_dim(out, b, i, 0)
    cur = b
    for s in range(1, n):
        cur = lax.ppermute(cur, ax, perm)
        out = lax.dynamic_update_index_in_dim(out, cur, (i - d * s) % n, 0)
    return out


def direct_ag(b, ax, n):
    i = lax.axis_index(ax)
    out = jnp.zeros((n,) + b.shape, b.dtype)
    out = lax.dynamic_update_index_in_dim(out, b, i, 0)
    for s in range(1, n):
        perm = [(j, (j + s) % n) for j in range(n)]
        out = lax.dynamic_update_index_in_dim(out, lax.ppermute(b, ax, perm), (i - s) % n, 0)
    return out


def direct_rs(blocks, ax, n):
    i = lax.axis_index(ax)
    acc = lax.dynamic_index_in_dim(blocks, i, 0, keepdims=False).astype(jnp.float32)
    for s in range(1, n):
        perm = [(j, (j + s) % n) for j in range(n)]
        send = lax.dynamic_index_in_dim(blocks, (i + s) % n, 0, keepdims=False)
        acc = acc + lax.ppermute(send, ax, perm).astype(jnp.float32)
    return acc


def to_ring_order(a):
    a5 = a.reshape(4, 4, 4, 16, a.shape[-1])
    pieces = []
    for q in range(4):
        piece = a5[:, :, q]
        if q >= 2:
            piece = piece.transpose(1, 0, 2, 3)
        pieces.append(piece.reshape(256, a.shape[-1]))
    return jnp.concatenate(pieces, 0)


def from_ring_order(a):
    pieces = []
    for q in range(4):
        piece = a[q * 256:(q + 1) * 256].reshape(4, 4, 16, a.shape[-1])
        if q >= 2:
            piece = piece.transpose(1, 0, 2, 3)
        pieces.append(piece)
    return jnp.stack(pieces, 2).reshape(a.shape)


def ring_scatter_col(a):
    qs = a.reshape(4, 4, 4, 16, a.shape[-1])
    r = [ring_rs(qs[q], "x" if q < 2 else "y", 4, 1 if q % 2 == 0 else -1) for q in range(4)]
    low = ring_rs(jnp.stack(r[:2], 1), "y", 4, 1)
    high = ring_rs(jnp.stack(r[2:], 1), "x", 4, -1)
    return jnp.concatenate([low, high], 0).reshape(64, a.shape[-1])


def ring_gather_col(b):
    parts = b.reshape(2, 2, 16, b.shape[-1])
    low = ring_ag(parts[0], "y", 4, 1)
    high = ring_ag(parts[1], "x", 4, -1)
    outs = []
    for q in range(4):
        g = (low if q < 2 else high)[:, q % 2]
        g = ring_ag(g, "x" if q < 2 else "y", 4, 1 if q % 2 == 0 else -1)
        outs.append(g.reshape(256, b.shape[-1]))
    return jnp.concatenate(outs, 0)


def gather_row(b):
    g = direct_ag(b, "core", 2)
    g = direct_ag(g, "z", 4)
    return g.reshape((-1, b.shape[-1]))


def scatter_row(part):
    p4 = part.reshape(4, 2, part.shape[0] // 8, part.shape[-1])
    acc = direct_rs(p4, "z", 4)
    c = lax.axis_index("core")
    mine = lax.dynamic_index_in_dim(acc, c, 0, keepdims=False)
    other = lax.dynamic_index_in_dim(acc, 1 - c, 0, keepdims=False)
    return (mine + lax.ppermute(other, "core", [(0, 1), (1, 0)])).astype(jnp.bfloat16)


def shards(page_tokens, weight_in, weight_out, upstream):
    width = page_tokens.shape[1]
    both = gather_row(jnp.concatenate([page_tokens, upstream], 1))
    features = both[:, :width]
    upstream_all = both[:, width:]
    hidden_pre = lax.psum_scatter(
        jnp.dot(features, weight_in, preferred_element_type=jnp.float32).astype(jnp.bfloat16),
        COL,
        scatter_dimension=0,
        tiled=True,
    ).astype(jnp.float32)
    grad_active = ring_scatter_col(
        contract_last(to_ring_order(upstream_all), weight_out).astype(jnp.bfloat16)
    ).astype(jnp.float32)
    active_loc = activate(hidden_pre).astype(jnp.bfloat16)
    split = active_loc.shape[1] // 2
    active_lo = lax.all_gather(active_loc[:, :split], COL, axis=0, tiled=True)
    active_hi = lax.all_gather(active_loc[:, split:], COL, axis=0, tiled=True)
    grad_hidden = ring_gather_col(activate_back(hidden_pre, grad_active).astype(jnp.bfloat16))
    out_part = (
        jnp.dot(active_lo, weight_out[:split], preferred_element_type=jnp.float32)
        + jnp.dot(active_hi, weight_out[split:], preferred_element_type=jnp.float32)
    ).astype(jnp.bfloat16)
    tokens_part = from_ring_order(contract_last(grad_hidden, weight_in).astype(jnp.bfloat16))
    outs = scatter_row(jnp.concatenate([out_part, tokens_part], 1))
    block_out = outs[:, :width]
    grad_tokens = outs[:, width:]
    grad_weight_in = contract_first(to_ring_order(features), grad_hidden).astype(jnp.bfloat16)
    grad_weight_out = jnp.concatenate(
        [contract_first(active_lo, upstream_all), contract_first(active_hi, upstream_all)], 0
    ).astype(jnp.bfloat16)
    return (block_out, grad_tokens, grad_weight_in, grad_weight_out)


def solution(mesh):
    grid = Mesh(mesh.devices.reshape(mesh.shape["row"] // 2, 2, 4, mesh.shape["col"] // 4), ROW + COL)
    tok = P(ROW, COL)
    return jax.shard_map(
        shards,
        mesh=grid,
        in_specs=(tok, P(COL, ROW), tok, tok),
        out_specs=(tok, tok, P(COL, ROW), tok),
        check_vma=False,
    )
```

```python
import jax
import jax.numpy as jnp
from jax import lax
from jax.sharding import Mesh
from jax.sharding import PartitionSpec as P

ROW = ("z", "core")
COL = ("x", "y")


def activate(values):
    return (
        0.5
        * values
        * (1.0 + jnp.tanh(0.7978845608 * (values + 0.044715 * values * values * values)))
    )


def activate_back(values, grads):
    return jax.vjp(activate, values)[1](grads)[0]


def contract_last(left, right):
    return lax.dot_general(
        left, right, (((1,), (1,)), ((), ())), preferred_element_type=jnp.float32
    )


def contract_first(left, right):
    return lax.dot_general(
        left, right, (((0,), (0,)), ((), ())), preferred_element_type=jnp.float32
    )


def ring_rs(blocks, ax, n, d):
    i = lax.axis_index(ax)
    perm = [(j, (j + d) % n) for j in range(n)]
    acc = lax.dynamic_index_in_dim(blocks, (i - d) % n, 0, keepdims=False)
    for s in range(1, n):
        acc = lax.ppermute(acc, ax, perm)
        acc = acc + lax.dynamic_index_in_dim(blocks, (i - d * (s + 1)) % n, 0, keepdims=False)
    return acc


def ring_ag(b, ax, n, d):
    i = lax.axis_index(ax)
    perm = [(j, (j + d) % n) for j in range(n)]
    out = jnp.zeros((n,) + b.shape, b.dtype)
    out = lax.dynamic_update_index_in_dim(out, b, i, 0)
    cur = b
    for s in range(1, n):
        cur = lax.ppermute(cur, ax, perm)
        out = lax.dynamic_update_index_in_dim(out, cur, (i - d * s) % n, 0)
    return out


def direct_ag(b, ax, n):
    i = lax.axis_index(ax)
    out = jnp.zeros((n,) + b.shape, b.dtype)
    out = lax.dynamic_update_index_in_dim(out, b, i, 0)
    for s in range(1, n):
        perm = [(j, (j + s) % n) for j in range(n)]
        out = lax.dynamic_update_index_in_dim(out, lax.ppermute(b, ax, perm), (i - s) % n, 0)
    return out


def direct_rs(blocks, ax, n):
    i = lax.axis_index(ax)
    acc = lax.dynamic_index_in_dim(blocks, i, 0, keepdims=False).astype(jnp.float32)
    for s in range(1, n):
        perm = [(j, (j + s) % n) for j in range(n)]
        send = lax.dynamic_index_in_dim(blocks, (i + s) % n, 0, keepdims=False)
        acc = acc + lax.ppermute(send, ax, perm).astype(jnp.float32)
    return acc


def to_ring_order(a):
    a5 = a.reshape(4, 4, 4, 16, a.shape[-1])
    pieces = []
    for q in range(4):
        piece = a5[:, :, q]
        if q >= 2:
            piece = piece.transpose(1, 0, 2, 3)
        pieces.append(piece.reshape(256, a.shape[-1]))
    return jnp.concatenate(pieces, 0)


def from_ring_order(a):
    pieces = []
    for q in range(4):
        piece = a[q * 256:(q + 1) * 256].reshape(4, 4, 16, a.shape[-1])
        if q >= 2:
            piece = piece.transpose(1, 0, 2, 3)
        pieces.append(piece)
    return jnp.stack(pieces, 2).reshape(a.shape)


def ring_scatter_col(a):
    qs = a.reshape(4, 4, 4, 16, a.shape[-1])
    r = [ring_rs(qs[q], "x" if q < 2 else "y", 4, 1 if q % 2 == 0 else -1) for q in range(4)]
    low = ring_rs(jnp.stack(r[:2], 1), "y", 4, 1)
    high = ring_rs(jnp.stack(r[2:], 1), "x", 4, -1)
    return jnp.concatenate([low, high], 0).reshape(64, a.shape[-1])


def ring_gather_col(b):
    parts = b.reshape(2, 2, 16, b.shape[-1])
    low = ring_ag(parts[0], "y", 4, 1)
    high = ring_ag(parts[1], "x", 4, -1)
    outs = []
    for q in range(4):
        g = (low if q < 2 else high)[:, q % 2]
        g = ring_ag(g, "x" if q < 2 else "y", 4, 1 if q % 2 == 0 else -1)
        outs.append(g.reshape(256, b.shape[-1]))
    return jnp.concatenate(outs, 0)


def gather_row(b):
    g = direct_ag(b, "core", 2)
    g = direct_ag(g, "z", 4)
    return g.reshape((-1, b.shape[-1]))


def scatter_row(part):
    p4 = part.reshape(4, 2, part.shape[0] // 8, part.shape[-1])
    acc = direct_rs(p4, "z", 4)
    c = lax.axis_index("core")
    mine = lax.dynamic_index_in_dim(acc, c, 0, keepdims=False)
    other = lax.dynamic_index_in_dim(acc, 1 - c, 0, keepdims=False)
    return (mine + lax.ppermute(other, "core", [(0, 1), (1, 0)])).astype(jnp.bfloat16)


def shards(page_tokens, weight_in, weight_out, upstream):
    width = page_tokens.shape[1]
    both = gather_row(jnp.concatenate([page_tokens, upstream], 1))
    features = both[:, :width]
    upstream_all = both[:, width:]
    both_ring = to_ring_order(both)
    hidden_pre = ring_scatter_col(
        jnp.dot(both_ring[:, :width], weight_in, preferred_element_type=jnp.float32).astype(jnp.bfloat16)
    ).astype(jnp.float32)
    grad_active = lax.psum_scatter(
        contract_last(upstream_all, weight_out).astype(jnp.bfloat16),
        COL,
        scatter_dimension=0,
        tiled=True,
    ).astype(jnp.float32)
    active = ring_gather_col(activate(hidden_pre).astype(jnp.bfloat16))
    grad_hidden = lax.all_gather(
        activate_back(hidden_pre, grad_active).astype(jnp.bfloat16), COL, axis=0, tiled=True
    )
    out_part = from_ring_order(
        jnp.dot(active, weight_out, preferred_element_type=jnp.float32).astype(jnp.bfloat16)
    )
    tokens_part = contract_last(grad_hidden, weight_in).astype(jnp.bfloat16)
    outs = scatter_row(jnp.concatenate([out_part, tokens_part], 1))
    block_out = outs[:, :width]
    grad_tokens = outs[:, width:]
    grad_weight_in = contract_first(features, grad_hidden).astype(jnp.bfloat16)
    grad_weight_out = contract_first(active, both_ring[:, width:]).astype(jnp.bfloat16)
    return (block_out, grad_tokens, grad_weight_in, grad_weight_out)


def solution(mesh):
    grid = Mesh(mesh.devices.reshape(mesh.shape["row"] // 2, 2, 4, mesh.shape["col"] // 4), ROW + COL)
    tok = P(ROW, COL)
    return jax.shard_map(
        shards,
        mesh=grid,
        in_specs=(tok, P(COL, ROW), tok, tok),
        out_specs=(tok, tok, P(COL, ROW), tok),
        check_vma=False,
    )
```

```python
import jax
import jax.numpy as jnp
from jax import lax
from jax.sharding import Mesh
from jax.sharding import PartitionSpec as P

ROW = ("z", "core")
COL = ("x", "y")


def activate(values):
    return (
        0.5
        * values
        * (1.0 + jnp.tanh(0.7978845608 * (values + 0.044715 * values * values * values)))
    )


def activate_back(values, grads):
    return jax.vjp(activate, values)[1](grads)[0]


def contract_last(left, right):
    return lax.dot_general(
        left, right, (((1,), (1,)), ((), ())), preferred_element_type=jnp.float32
    )


def contract_first(left, right):
    return lax.dot_general(
        left, right, (((0,), (0,)), ((), ())), preferred_element_type=jnp.float32
    )


def ring_rs(blocks, ax, n, d):
    i = lax.axis_index(ax)
    perm = [(j, (j + d) % n) for j in range(n)]
    acc = lax.dynamic_index_in_dim(blocks, (i - d) % n, 0, keepdims=False)
    for s in range(1, n):
        acc = lax.ppermute(acc, ax, perm)
        acc = acc + lax.dynamic_index_in_dim(blocks, (i - d * (s + 1)) % n, 0, keepdims=False)
    return acc


def ring_ag(b, ax, n, d):
    i = lax.axis_index(ax)
    perm = [(j, (j + d) % n) for j in range(n)]
    out = jnp.zeros((n,) + b.shape, b.dtype)
    out = lax.dynamic_update_index_in_dim(out, b, i, 0)
    cur = b
    for s in range(1, n):
        cur = lax.ppermute(cur, ax, perm)
        out = lax.dynamic_update_index_in_dim(out, cur, (i - d * s) % n, 0)
    return out


def direct_ag(b, ax, n):
    i = lax.axis_index(ax)
    out = jnp.zeros((n,) + b.shape, b.dtype)
    out = lax.dynamic_update_index_in_dim(out, b, i, 0)
    for s in range(1, n):
        perm = [(j, (j + s) % n) for j in range(n)]
        out = lax.dynamic_update_index_in_dim(out, lax.ppermute(b, ax, perm), (i - s) % n, 0)
    return out


def direct_rs(blocks, ax, n):
    i = lax.axis_index(ax)
    acc = lax.dynamic_index_in_dim(blocks, i, 0, keepdims=False).astype(jnp.float32)
    for s in range(1, n):
        perm = [(j, (j + s) % n) for j in range(n)]
        send = lax.dynamic_index_in_dim(blocks, (i + s) % n, 0, keepdims=False)
        acc = acc + lax.ppermute(send, ax, perm).astype(jnp.float32)
    return acc


def to_ring_order(a):
    a5 = a.reshape(4, 4, 4, 16, a.shape[-1])
    pieces = []
    for q in range(4):
        piece = a5[:, :, q]
        if q >= 2:
            piece = piece.transpose(1, 0, 2, 3)
        pieces.append(piece.reshape(256, a.shape[-1]))
    return jnp.concatenate(pieces, 0)


def from_ring_order(a):
    pieces = []
    for q in range(4):
        piece = a[q * 256:(q + 1) * 256].reshape(4, 4, 16, a.shape[-1])
        if q >= 2:
            piece = piece.transpose(1, 0, 2, 3)
        pieces.append(piece)
    return jnp.stack(pieces, 2).reshape(a.shape)


def ring_scatter_col(a):
    qs = a.reshape(4, 4, 4, 16, a.shape[-1])
    r = [ring_rs(qs[q], "x" if q < 2 else "y", 4, 1 if q % 2 == 0 else -1) for q in range(4)]
    low = ring_rs(jnp.stack(r[:2], 1), "y", 4, 1)
    high = ring_rs(jnp.stack(r[2:], 1), "x", 4, -1)
    return jnp.concatenate([low, high], 0).reshape(64, a.shape[-1])


def ring_gather_col(b):
    parts = b.reshape(2, 2, 16, b.shape[-1])
    low = ring_ag(parts[0], "y", 4, 1)
    high = ring_ag(parts[1], "x", 4, -1)
    outs = []
    for q in range(4):
        g = (low if q < 2 else high)[:, q % 2]
        g = ring_ag(g, "x" if q < 2 else "y", 4, 1 if q % 2 == 0 else -1)
        outs.append(g.reshape(256, b.shape[-1]))
    return jnp.concatenate(outs, 0)


def gather_row(b):
    g = direct_ag(b, "core", 2)
    g = direct_ag(g, "z", 4)
    return g.reshape((-1, b.shape[-1]))


def scatter_row(part):
    p4 = part.reshape(4, 2, part.shape[0] // 8, part.shape[-1])
    acc = direct_rs(p4, "z", 4)
    c = lax.axis_index("core")
    mine = lax.dynamic_index_in_dim(acc, c, 0, keepdims=False)
    other = lax.dynamic_index_in_dim(acc, 1 - c, 0, keepdims=False)
    return (mine + lax.ppermute(other, "core", [(0, 1), (1, 0)])).astype(jnp.bfloat16)


def shards(page_tokens, weight_in, weight_out, upstream):
    width = page_tokens.shape[1]
    both = lax.all_gather(jnp.concatenate([page_tokens, upstream], 1), ROW, axis=0, tiled=True)
    features = both[:, :width]
    upstream_all = both[:, width:]
    both_ring = to_ring_order(both)
    hidden_pre = ring_scatter_col(
        jnp.dot(both_ring[:, :width], weight_in, preferred_element_type=jnp.float32).astype(jnp.bfloat16)
    ).astype(jnp.float32)
    grad_active = lax.psum_scatter(
        contract_last(upstream_all, weight_out).astype(jnp.bfloat16),
        COL,
        scatter_dimension=0,
        tiled=True,
    ).astype(jnp.float32)
    active = ring_gather_col(activate(hidden_pre).astype(jnp.bfloat16))
    grad_hidden = lax.all_gather(
        activate_back(hidden_pre, grad_active).astype(jnp.bfloat16), COL, axis=0, tiled=True
    )
    out_part = from_ring_order(
        jnp.dot(active, weight_out, preferred_element_type=jnp.float32).astype(jnp.bfloat16)
    )
    tokens_part = contract_last(grad_hidden, weight_in).astype(jnp.bfloat16)
    outs = scatter_row(jnp.concatenate([out_part, tokens_part], 1))
    block_out = outs[:, :width]
    grad_tokens = outs[:, width:]
    grad_weight_in = contract_first(features, grad_hidden).astype(jnp.bfloat16)
    grad_weight_out = contract_first(active, both_ring[:, width:]).astype(jnp.bfloat16)
    return (block_out, grad_tokens, grad_weight_in, grad_weight_out)


def solution(mesh):
    grid = Mesh(mesh.devices.reshape(mesh.shape["row"] // 2, 2, 4, mesh.shape["col"] // 4), ROW + COL)
    tok = P(ROW, COL)
    return jax.shard_map(
        shards,
        mesh=grid,
        in_specs=(tok, P(COL, ROW), tok, tok),
        out_specs=(tok, tok, P(COL, ROW), tok),
        check_vma=False,
    )
```

```python
import jax
import jax.numpy as jnp
from jax import lax
from jax.sharding import Mesh
from jax.sharding import PartitionSpec as P

ROW = ("z", "core")
COL = ("x", "y")


def activate(values):
    return (
        0.5
        * values
        * (1.0 + jnp.tanh(0.7978845608 * (values + 0.044715 * values * values * values)))
    )


def activate_back(values, grads):
    return jax.vjp(activate, values)[1](grads)[0]


def contract_last(left, right):
    return lax.dot_general(
        left, right, (((1,), (1,)), ((), ())), preferred_element_type=jnp.float32
    )


def contract_first(left, right):
    return lax.dot_general(
        left, right, (((0,), (0,)), ((), ())), preferred_element_type=jnp.float32
    )


def ring_rs(blocks, ax, n, d):
    i = lax.axis_index(ax)
    perm = [(j, (j + d) % n) for j in range(n)]
    acc = lax.dynamic_index_in_dim(blocks, (i - d) % n, 0, keepdims=False)
    for s in range(1, n):
        acc = lax.ppermute(acc, ax, perm)
        acc = acc + lax.dynamic_index_in_dim(blocks, (i - d * (s + 1)) % n, 0, keepdims=False)
    return acc


def ring_ag(b, ax, n, d):
    i = lax.axis_index(ax)
    perm = [(j, (j + d) % n) for j in range(n)]
    out = jnp.zeros((n,) + b.shape, b.dtype)
    out = lax.dynamic_update_index_in_dim(out, b, i, 0)
    cur = b
    for s in range(1, n):
        cur = lax.ppermute(cur, ax, perm)
        out = lax.dynamic_update_index_in_dim(out, cur, (i - d * s) % n, 0)
    return out


def direct_ag(b, ax, n):
    i = lax.axis_index(ax)
    out = jnp.zeros((n,) + b.shape, b.dtype)
    out = lax.dynamic_update_index_in_dim(out, b, i, 0)
    for s in range(1, n):
        perm = [(j, (j + s) % n) for j in range(n)]
        out = lax.dynamic_update_index_in_dim(out, lax.ppermute(b, ax, perm), (i - s) % n, 0)
    return out


def direct_rs(blocks, ax, n):
    i = lax.axis_index(ax)
    acc = lax.dynamic_index_in_dim(blocks, i, 0, keepdims=False).astype(jnp.float32)
    for s in range(1, n):
        perm = [(j, (j + s) % n) for j in range(n)]
        send = lax.dynamic_index_in_dim(blocks, (i + s) % n, 0, keepdims=False)
        acc = acc + lax.ppermute(send, ax, perm).astype(jnp.float32)
    return acc


def to_ring_order(a):
    a5 = a.reshape(4, 4, 4, 16, a.shape[-1])
    pieces = []
    for q in range(4):
        piece = a5[:, :, q]
        if q >= 2:
            piece = piece.transpose(1, 0, 2, 3)
        pieces.append(piece.reshape(256, a.shape[-1]))
    return jnp.concatenate(pieces, 0)


def from_ring_order(a):
    pieces = []
    for q in range(4):
        piece = a[q * 256:(q + 1) * 256].reshape(4, 4, 16, a.shape[-1])
        if q >= 2:
            piece = piece.transpose(1, 0, 2, 3)
        pieces.append(piece)
    return jnp.stack(pieces, 2).reshape(a.shape)


def ring_scatter_col(a):
    qs = a.reshape(4, 4, 4, 16, a.shape[-1])
    r = [ring_rs(qs[q], "x" if q < 2 else "y", 4, 1 if q % 2 == 0 else -1) for q in range(4)]
    low = ring_rs(jnp.stack(r[:2], 1), "y", 4, 1)
    high = ring_rs(jnp.stack(r[2:], 1), "x", 4, -1)
    return jnp.concatenate([low, high], 0).reshape(64, a.shape[-1])


def ring_gather_col(b):
    parts = b.reshape(2, 2, 16, b.shape[-1])
    low = ring_ag(parts[0], "y", 4, 1)
    high = ring_ag(parts[1], "x", 4, -1)
    outs = []
    for q in range(4):
        g = (low if q < 2 else high)[:, q % 2]
        g = ring_ag(g, "x" if q < 2 else "y", 4, 1 if q % 2 == 0 else -1)
        outs.append(g.reshape(256, b.shape[-1]))
    return jnp.concatenate(outs, 0)


def gather_row(b):
    g = direct_ag(b, "core", 2)
    g = direct_ag(g, "z", 4)
    return g.reshape((-1, b.shape[-1]))


def scatter_row(part):
    p4 = part.reshape(4, 2, part.shape[0] // 8, part.shape[-1])
    acc = direct_rs(p4, "z", 4)
    c = lax.axis_index("core")
    mine = lax.dynamic_index_in_dim(acc, c, 0, keepdims=False)
    other = lax.dynamic_index_in_dim(acc, 1 - c, 0, keepdims=False)
    return (mine + lax.ppermute(other, "core", [(0, 1), (1, 0)])).astype(jnp.bfloat16)


def shards(page_tokens, weight_in, weight_out, upstream):
    width = page_tokens.shape[1]
    both = lax.all_gather(jnp.concatenate([page_tokens, upstream], 1), ROW, axis=0, tiled=True)
    features = both[:, :width]
    upstream_all = both[:, width:]
    both_ring = to_ring_order(both)
    grad_part = contract_last(upstream_all, weight_out).astype(jnp.bfloat16)
    grad_part, features_ring = lax.optimization_barrier((grad_part, both_ring[:, :width]))
    hidden_pre = ring_scatter_col(
        jnp.dot(features_ring, weight_in, preferred_element_type=jnp.float32).astype(jnp.bfloat16)
    ).astype(jnp.float32)
    grad_active = lax.psum_scatter(
        grad_part,
        COL,
        scatter_dimension=0,
        tiled=True,
    ).astype(jnp.float32)
    active = ring_gather_col(activate(hidden_pre).astype(jnp.bfloat16))
    grad_hidden = lax.all_gather(
        activate_back(hidden_pre, grad_active).astype(jnp.bfloat16), COL, axis=0, tiled=True
    )
    out_part = from_ring_order(
        jnp.dot(active, weight_out, preferred_element_type=jnp.float32).astype(jnp.bfloat16)
    )
    tokens_part = contract_last(grad_hidden, weight_in).astype(jnp.bfloat16)
    outs = scatter_row(jnp.concatenate([out_part, tokens_part], 1))
    block_out = outs[:, :width]
    grad_tokens = outs[:, width:]
    grad_weight_in = contract_first(features, grad_hidden).astype(jnp.bfloat16)
    grad_weight_out = contract_first(active, both_ring[:, width:]).astype(jnp.bfloat16)
    return (block_out, grad_tokens, grad_weight_in, grad_weight_out)


def solution(mesh):
    grid = Mesh(mesh.devices.reshape(mesh.shape["row"] // 2, 2, 4, mesh.shape["col"] // 4), ROW + COL)
    tok = P(ROW, COL)
    return jax.shard_map(
        shards,
        mesh=grid,
        in_specs=(tok, P(COL, ROW), tok, tok),
        out_specs=(tok, tok, P(COL, ROW), tok),
        check_vma=False,
    )
```

```python
import jax
import jax.numpy as jnp
from jax import lax
from jax.sharding import Mesh
from jax.sharding import PartitionSpec as P

ROW = ("z", "core")
COL = ("x", "y")


def activate(values):
    return (
        0.5
        * values
        * (1.0 + jnp.tanh(0.7978845608 * (values + 0.044715 * values * values * values)))
    )


def activate_back(values, grads):
    return jax.vjp(activate, values)[1](grads)[0]


def contract_last(left, right):
    return lax.dot_general(
        left, right, (((1,), (1,)), ((), ())), preferred_element_type=jnp.float32
    )


def contract_first(left, right):
    return lax.dot_general(
        left, right, (((0,), (0,)), ((), ())), preferred_element_type=jnp.float32
    )


def ring_rs(blocks, ax, n, d):
    i = lax.axis_index(ax)
    perm = [(j, (j + d) % n) for j in range(n)]
    acc = lax.dynamic_index_in_dim(blocks, (i - d) % n, 0, keepdims=False)
    for s in range(1, n):
        acc = lax.ppermute(acc, ax, perm)
        acc = acc + lax.dynamic_index_in_dim(blocks, (i - d * (s + 1)) % n, 0, keepdims=False)
    return acc


def ring_ag(b, ax, n, d):
    i = lax.axis_index(ax)
    perm = [(j, (j + d) % n) for j in range(n)]
    out = jnp.zeros((n,) + b.shape, b.dtype)
    out = lax.dynamic_update_index_in_dim(out, b, i, 0)
    cur = b
    for s in range(1, n):
        cur = lax.ppermute(cur, ax, perm)
        out = lax.dynamic_update_index_in_dim(out, cur, (i - d * s) % n, 0)
    return out


def direct_ag(b, ax, n):
    i = lax.axis_index(ax)
    out = jnp.zeros((n,) + b.shape, b.dtype)
    out = lax.dynamic_update_index_in_dim(out, b, i, 0)
    for s in range(1, n):
        perm = [(j, (j + s) % n) for j in range(n)]
        out = lax.dynamic_update_index_in_dim(out, lax.ppermute(b, ax, perm), (i - s) % n, 0)
    return out


def direct_rs(blocks, ax, n):
    i = lax.axis_index(ax)
    acc = lax.dynamic_index_in_dim(blocks, i, 0, keepdims=False).astype(jnp.float32)
    for s in range(1, n):
        perm = [(j, (j + s) % n) for j in range(n)]
        send = lax.dynamic_index_in_dim(blocks, (i + s) % n, 0, keepdims=False)
        acc = acc + lax.ppermute(send, ax, perm).astype(jnp.float32)
    return acc


def to_ring_order(a):
    a5 = a.reshape(4, 4, 4, 16, a.shape[-1])
    pieces = []
    for q in range(4):
        piece = a5[:, :, q]
        if q >= 2:
            piece = piece.transpose(1, 0, 2, 3)
        pieces.append(piece.reshape(256, a.shape[-1]))
    return jnp.concatenate(pieces, 0)


def from_ring_order(a):
    pieces = []
    for q in range(4):
        piece = a[q * 256:(q + 1) * 256].reshape(4, 4, 16, a.shape[-1])
        if q >= 2:
            piece = piece.transpose(1, 0, 2, 3)
        pieces.append(piece)
    return jnp.stack(pieces, 2).reshape(a.shape)


def ring_scatter_col(a):
    qs = a.reshape(4, 4, 4, 16, a.shape[-1])
    r = [ring_rs(qs[q], "x" if q < 2 else "y", 4, 1 if q % 2 == 0 else -1) for q in range(4)]
    low = ring_rs(jnp.stack(r[:2], 1), "y", 4, 1)
    high = ring_rs(jnp.stack(r[2:], 1), "x", 4, -1)
    return jnp.concatenate([low, high], 0).reshape(64, a.shape[-1])


def ring_gather_col(b):
    parts = b.reshape(2, 2, 16, b.shape[-1])
    low = ring_ag(parts[0], "y", 4, 1)
    high = ring_ag(parts[1], "x", 4, -1)
    outs = []
    for q in range(4):
        g = (low if q < 2 else high)[:, q % 2]
        g = ring_ag(g, "x" if q < 2 else "y", 4, 1 if q % 2 == 0 else -1)
        outs.append(g.reshape(256, b.shape[-1]))
    return jnp.concatenate(outs, 0)


def gather_row(b):
    g = direct_ag(b, "core", 2)
    g = direct_ag(g, "z", 4)
    return g.reshape((-1, b.shape[-1]))


def scatter_row(part):
    p4 = part.reshape(4, 2, part.shape[0] // 8, part.shape[-1])
    acc = direct_rs(p4, "z", 4)
    c = lax.axis_index("core")
    mine = lax.dynamic_index_in_dim(acc, c, 0, keepdims=False)
    other = lax.dynamic_index_in_dim(acc, 1 - c, 0, keepdims=False)
    return (mine + lax.ppermute(other, "core", [(0, 1), (1, 0)])).astype(jnp.bfloat16)


def shards(page_tokens, weight_in, weight_out, upstream):
    width = page_tokens.shape[1]
    both = lax.all_gather(jnp.concatenate([page_tokens, upstream], 1), ROW, axis=0, tiled=True)
    features = both[:, :width]
    upstream_all = both[:, width:]
    both_ring = to_ring_order(both)
    hidden_pre = ring_scatter_col(
        jnp.dot(both_ring[:, :width], weight_in, preferred_element_type=jnp.float32).astype(jnp.bfloat16)
    ).astype(jnp.float32)
    grad_active = lax.psum_scatter(
        contract_last(upstream_all, weight_out).astype(jnp.bfloat16),
        COL,
        scatter_dimension=0,
        tiled=True,
    ).astype(jnp.float32)
    active = ring_gather_col(activate(hidden_pre).astype(jnp.bfloat16))
    grad_hidden = lax.all_gather(
        activate_back(hidden_pre, grad_active).astype(jnp.bfloat16), COL, axis=0, tiled=True
    )
    out_part = from_ring_order(
        jnp.dot(active, weight_out, preferred_element_type=jnp.float32).astype(jnp.bfloat16)
    )
    tokens_part = contract_last(grad_hidden, weight_in).astype(jnp.bfloat16)
    outs = lax.psum_scatter(jnp.concatenate([out_part, tokens_part], 1), ROW, scatter_dimension=0, tiled=True)
    block_out = outs[:, :width]
    grad_tokens = outs[:, width:]
    grad_weight_in = contract_first(features, grad_hidden).astype(jnp.bfloat16)
    grad_weight_out = contract_first(active, both_ring[:, width:]).astype(jnp.bfloat16)
    return (block_out, grad_tokens, grad_weight_in, grad_weight_out)


def solution(mesh):
    grid = Mesh(mesh.devices.reshape(mesh.shape["row"] // 2, 2, 4, mesh.shape["col"] // 4), ROW + COL)
    tok = P(ROW, COL)
    return jax.shard_map(
        shards,
        mesh=grid,
        in_specs=(tok, P(COL, ROW), tok, tok),
        out_specs=(tok, tok, P(COL, ROW), tok),
        check_vma=False,
    )
```

```python
import jax
import jax.numpy as jnp
from jax import lax
from jax.sharding import Mesh
from jax.sharding import PartitionSpec as P

ROW = ("z", "core")
COL = ("x", "y")


def activate(values):
    return (
        0.5
        * values
        * (1.0 + jnp.tanh(0.7978845608 * (values + 0.044715 * values * values * values)))
    )


def activate_back(values, grads):
    return jax.vjp(activate, values)[1](grads)[0]


def contract_last(left, right):
    return lax.dot_general(
        left, right, (((1,), (1,)), ((), ())), preferred_element_type=jnp.float32
    )


def contract_first(left, right):
    return lax.dot_general(
        left, right, (((0,), (0,)), ((), ())), preferred_element_type=jnp.float32
    )


def ring_rs(blocks, ax, n, d):
    i = lax.axis_index(ax)
    perm = [(j, (j + d) % n) for j in range(n)]
    acc = lax.dynamic_index_in_dim(blocks, (i - d) % n, 0, keepdims=False)
    for s in range(1, n):
        acc = lax.ppermute(acc, ax, perm)
        acc = acc + lax.dynamic_index_in_dim(blocks, (i - d * (s + 1)) % n, 0, keepdims=False)
    return acc


def ring_ag(b, ax, n, d):
    i = lax.axis_index(ax)
    perm = [(j, (j + d) % n) for j in range(n)]
    out = jnp.zeros((n,) + b.shape, b.dtype)
    out = lax.dynamic_update_index_in_dim(out, b, i, 0)
    cur = b
    for s in range(1, n):
        cur = lax.ppermute(cur, ax, perm)
        out = lax.dynamic_update_index_in_dim(out, cur, (i - d * s) % n, 0)
    return out


def direct_ag(b, ax, n):
    i = lax.axis_index(ax)
    out = jnp.zeros((n,) + b.shape, b.dtype)
    out = lax.dynamic_update_index_in_dim(out, b, i, 0)
    for s in range(1, n):
        perm = [(j, (j + s) % n) for j in range(n)]
        out = lax.dynamic_update_index_in_dim(out, lax.ppermute(b, ax, perm), (i - s) % n, 0)
    return out


def direct_rs(blocks, ax, n):
    i = lax.axis_index(ax)
    acc = lax.dynamic_index_in_dim(blocks, i, 0, keepdims=False).astype(jnp.float32)
    for s in range(1, n):
        perm = [(j, (j + s) % n) for j in range(n)]
        send = lax.dynamic_index_in_dim(blocks, (i + s) % n, 0, keepdims=False)
        acc = acc + lax.ppermute(send, ax, perm).astype(jnp.float32)
    return acc


def to_ring_order(a):
    a5 = a.reshape(4, 4, 4, 16, a.shape[-1])
    pieces = []
    for q in range(4):
        piece = a5[:, :, q]
        if q >= 2:
            piece = piece.transpose(1, 0, 2, 3)
        pieces.append(piece.reshape(256, a.shape[-1]))
    return jnp.concatenate(pieces, 0)


def from_ring_order(a):
    pieces = []
    for q in range(4):
        piece = a[q * 256:(q + 1) * 256].reshape(4, 4, 16, a.shape[-1])
        if q >= 2:
            piece = piece.transpose(1, 0, 2, 3)
        pieces.append(piece)
    return jnp.stack(pieces, 2).reshape(a.shape)


def ring_scatter_col(a):
    qs = a.reshape(4, 4, 4, 16, a.shape[-1])
    r = [ring_rs(qs[q], "x" if q < 2 else "y", 4, 1 if q % 2 == 0 else -1) for q in range(4)]
    low = ring_rs(jnp.stack(r[:2], 1), "y", 4, 1)
    high = ring_rs(jnp.stack(r[2:], 1), "x", 4, -1)
    return jnp.concatenate([low, high], 0).reshape(64, a.shape[-1])


def ring_gather_col(b):
    parts = b.reshape(2, 2, 16, b.shape[-1])
    low = ring_ag(parts[0], "y", 4, 1)
    high = ring_ag(parts[1], "x", 4, -1)
    outs = []
    for q in range(4):
        g = (low if q < 2 else high)[:, q % 2]
        g = ring_ag(g, "x" if q < 2 else "y", 4, 1 if q % 2 == 0 else -1)
        outs.append(g.reshape(256, b.shape[-1]))
    return jnp.concatenate(outs, 0)


def gather_row(b):
    g = direct_ag(b, "core", 2)
    g = direct_ag(g, "z", 4)
    return g.reshape((-1, b.shape[-1]))


def scatter_row(part):
    p4 = part.reshape(4, 2, part.shape[0] // 8, part.shape[-1])
    c = lax.axis_index("core")
    mine = lax.dynamic_index_in_dim(p4, c, 1, keepdims=False)
    other = lax.dynamic_index_in_dim(p4, 1 - c, 1, keepdims=False)
    pair = mine.astype(jnp.float32) + lax.ppermute(other, "core", [(0, 1), (1, 0)]).astype(jnp.float32)
    return direct_rs(pair.astype(jnp.bfloat16), "z", 4).astype(jnp.bfloat16)


def shards(page_tokens, weight_in, weight_out, upstream):
    width = page_tokens.shape[1]
    both = lax.all_gather(jnp.concatenate([page_tokens, upstream], 1), ROW, axis=0, tiled=True)
    features = both[:, :width]
    upstream_all = both[:, width:]
    both_ring = to_ring_order(both)
    hidden_pre = ring_scatter_col(
        jnp.dot(both_ring[:, :width], weight_in, preferred_element_type=jnp.float32).astype(jnp.bfloat16)
    ).astype(jnp.float32)
    grad_active = lax.psum_scatter(
        contract_last(upstream_all, weight_out).astype(jnp.bfloat16),
        COL,
        scatter_dimension=0,
        tiled=True,
    ).astype(jnp.float32)
    active = ring_gather_col(activate(hidden_pre).astype(jnp.bfloat16))
    grad_hidden = lax.all_gather(
        activate_back(hidden_pre, grad_active).astype(jnp.bfloat16), COL, axis=0, tiled=True
    )
    out_part = from_ring_order(
        jnp.dot(active, weight_out, preferred_element_type=jnp.float32).astype(jnp.bfloat16)
    )
    tokens_part = contract_last(grad_hidden, weight_in).astype(jnp.bfloat16)
    outs = scatter_row(jnp.concatenate([out_part, tokens_part], 1))
    block_out = outs[:, :width]
    grad_tokens = outs[:, width:]
    grad_weight_in = contract_first(features, grad_hidden).astype(jnp.bfloat16)
    grad_weight_out = contract_first(active, both_ring[:, width:]).astype(jnp.bfloat16)
    return (block_out, grad_tokens, grad_weight_in, grad_weight_out)


def solution(mesh):
    grid = Mesh(mesh.devices.reshape(mesh.shape["row"] // 2, 2, 4, mesh.shape["col"] // 4), ROW + COL)
    tok = P(ROW, COL)
    return jax.shard_map(
        shards,
        mesh=grid,
        in_specs=(tok, P(COL, ROW), tok, tok),
        out_specs=(tok, tok, P(COL, ROW), tok),
        check_vma=False,
    )
```

```python
import jax
import jax.numpy as jnp
from jax import lax
from jax.sharding import Mesh
from jax.sharding import PartitionSpec as P

ROW = ("z", "core")
COL = ("x", "y")


def activate(values):
    return (
        0.5
        * values
        * (1.0 + jnp.tanh(0.7978845608 * (values + 0.044715 * values * values * values)))
    )


def activate_back(values, grads):
    return jax.vjp(activate, values)[1](grads)[0]


def contract_last(left, right):
    return lax.dot_general(
        left, right, (((1,), (1,)), ((), ())), preferred_element_type=jnp.float32
    )


def contract_first(left, right):
    return lax.dot_general(
        left, right, (((0,), (0,)), ((), ())), preferred_element_type=jnp.float32
    )


def ring_rs(blocks, ax, n, d):
    i = lax.axis_index(ax)
    perm = [(j, (j + d) % n) for j in range(n)]
    acc = lax.dynamic_index_in_dim(blocks, (i - d) % n, 0, keepdims=False)
    for s in range(1, n):
        acc = lax.ppermute(acc, ax, perm)
        acc = acc + lax.dynamic_index_in_dim(blocks, (i - d * (s + 1)) % n, 0, keepdims=False)
    return acc


def ring_ag(b, ax, n, d):
    i = lax.axis_index(ax)
    perm = [(j, (j + d) % n) for j in range(n)]
    out = jnp.zeros((n,) + b.shape, b.dtype)
    out = lax.dynamic_update_index_in_dim(out, b, i, 0)
    cur = b
    for s in range(1, n):
        cur = lax.ppermute(cur, ax, perm)
        out = lax.dynamic_update_index_in_dim(out, cur, (i - d * s) % n, 0)
    return out


def direct_ag(b, ax, n):
    i = lax.axis_index(ax)
    out = jnp.zeros((n,) + b.shape, b.dtype)
    out = lax.dynamic_update_index_in_dim(out, b, i, 0)
    for s in range(1, n):
        perm = [(j, (j + s) % n) for j in range(n)]
        out = lax.dynamic_update_index_in_dim(out, lax.ppermute(b, ax, perm), (i - s) % n, 0)
    return out


def direct_rs(blocks, ax, n):
    i = lax.axis_index(ax)
    acc = lax.dynamic_index_in_dim(blocks, i, 0, keepdims=False).astype(jnp.float32)
    for s in range(1, n):
        perm = [(j, (j + s) % n) for j in range(n)]
        send = lax.dynamic_index_in_dim(blocks, (i + s) % n, 0, keepdims=False)
        acc = acc + lax.ppermute(send, ax, perm).astype(jnp.float32)
    return acc


def to_ring_order(a):
    a5 = a.reshape(4, 4, 4, 16, a.shape[-1])
    pieces = []
    for q in range(4):
        piece = a5[:, :, q]
        if q >= 2:
            piece = piece.transpose(1, 0, 2, 3)
        pieces.append(piece.reshape(256, a.shape[-1]))
    return jnp.concatenate(pieces, 0)


def from_ring_order(a):
    pieces = []
    for q in range(4):
        piece = a[q * 256:(q + 1) * 256].reshape(4, 4, 16, a.shape[-1])
        if q >= 2:
            piece = piece.transpose(1, 0, 2, 3)
        pieces.append(piece)
    return jnp.stack(pieces, 2).reshape(a.shape)


def ring_scatter_col(a):
    qs = a.reshape(4, 4, 4, 16, a.shape[-1])
    r = [ring_rs(qs[q], "x" if q < 2 else "y", 4, 1 if q % 2 == 0 else -1) for q in range(4)]
    low = ring_rs(jnp.stack(r[:2], 1), "y", 4, 1)
    high = ring_rs(jnp.stack(r[2:], 1), "x", 4, -1)
    return jnp.concatenate([low, high], 0).reshape(64, a.shape[-1])


def ring_gather_col(b):
    parts = b.reshape(2, 2, 16, b.shape[-1])
    low = ring_ag(parts[0], "y", 4, 1)
    high = ring_ag(parts[1], "x", 4, -1)
    outs = []
    for q in range(4):
        g = (low if q < 2 else high)[:, q % 2]
        g = ring_ag(g, "x" if q < 2 else "y", 4, 1 if q % 2 == 0 else -1)
        outs.append(g.reshape(256, b.shape[-1]))
    return jnp.concatenate(outs, 0)


def gather_row(b):
    g = direct_ag(b, "core", 2)
    g = direct_ag(g, "z", 4)
    return g.reshape((-1, b.shape[-1]))


def scatter_row(part):
    p4 = part.reshape(4, 2, part.shape[0] // 8, part.shape[-1])
    acc = direct_rs(p4, "z", 4)
    c = lax.axis_index("core")
    mine = lax.dynamic_index_in_dim(acc, c, 0, keepdims=False)
    other = lax.dynamic_index_in_dim(acc, 1 - c, 0, keepdims=False)
    return (mine + lax.ppermute(other, "core", [(0, 1), (1, 0)])).astype(jnp.bfloat16)


def shards(page_tokens, weight_in, weight_out, upstream):
    width = page_tokens.shape[1]
    both = lax.all_gather(jnp.concatenate([page_tokens, upstream], 1), ROW, axis=0, tiled=True)
    features = both[:, :width]
    upstream_all = both[:, width:]
    both_ring = to_ring_order(both)
    hidden_pre = ring_scatter_col(
        jnp.dot(both_ring[:, :width], weight_in, preferred_element_type=jnp.float32).astype(jnp.bfloat16)
    ).astype(jnp.float32)
    grad_active = lax.psum_scatter(
        contract_last(upstream_all, weight_out).astype(jnp.bfloat16),
        COL,
        scatter_dimension=0,
        tiled=True,
    ).astype(jnp.float32)
    active = ring_gather_col(activate(hidden_pre).astype(jnp.bfloat16))
    grad_hidden = lax.all_gather(
        activate_back(hidden_pre, grad_active).astype(jnp.bfloat16), COL, axis=0, tiled=True
    )
    out_part = from_ring_order(
        jnp.dot(active, weight_out, preferred_element_type=jnp.float32).astype(jnp.bfloat16)
    )
    tokens_part = contract_last(grad_hidden, weight_in).astype(jnp.bfloat16)
    block_out = scatter_row(out_part)
    grad_tokens = scatter_row(tokens_part)
    grad_weight_in = contract_first(features, grad_hidden).astype(jnp.bfloat16)
    grad_weight_out = contract_first(active, both_ring[:, width:]).astype(jnp.bfloat16)
    return (block_out, grad_tokens, grad_weight_in, grad_weight_out)


def solution(mesh):
    grid = Mesh(mesh.devices.reshape(mesh.shape["row"] // 2, 2, 4, mesh.shape["col"] // 4), ROW + COL)
    tok = P(ROW, COL)
    return jax.shard_map(
        shards,
        mesh=grid,
        in_specs=(tok, P(COL, ROW), tok, tok),
        out_specs=(tok, tok, P(COL, ROW), tok),
        check_vma=False,
    )
```
